256 devices in a mesh: row: 8 (over x, core), col: 32 (over y, z).
Axes of the slice: x: 4, y: 4, z: 8, core: 2. Of those that a mesh axis runs over, the one named last changes fastest.
Arguments:
- tokens: bfloat16 [512, 8192], P('col', 'row'), may hold values from -6 to 6
- cotangent: bfloat16 [512, 8192], P('col', 'row'), may hold values from -6 to 6
- gate_weight: bfloat16 [8192, 28672], P('row', 'col'), may hold values from -0.09375 to 0.09375
- up_weight: bfloat16 [8192, 28672], P('row', 'col'), may hold values from -0.09375 to 0.09375
- down_weight: bfloat16 [28672, 8192], P('col', 'row'), may hold values from -0.046875 to 0.046875
- block_mask: int32 [3, 64, 224], P(None, 'row', 'col'), may hold values 0 or 1
Outputs:
- layer_out: bfloat16 [512, 8192], P('col', 'row')
- token_grad: bfloat16 [512, 8192], P('col', 'row')
- gate_grad: bfloat16 [8192, 28672], P('row', 'col')
- up_grad: bfloat16 [8192, 28672], P('row', 'col')
- down_grad: bfloat16 [28672, 8192], P('col', 'row')
The draws below stay inside these ranges and needn't reach their ends.
All inputs are finite; a program needn't handle non-finite values. No bound on the sum of `block_mask` on one device may be relied on, other than what follows from the above.
Results may differ from the reference program's by a relative error of at most 0.025.
Values may be sent and summed in bfloat16 or wider, within the bound.
No kernel may reach another device: no remote copies, remote signals or barrier semaphores. Data moves between devices by JAX's collectives and lax.ppermute only.
A program may use at most 64 MiB of HBM per device.

```python
import jax
import jax.numpy as jnp
from jax import lax

D = 8192
FF = 28672
BLOCK = 128
TOKENS = 512
N_ROW = 8
N_COL = 32


def set_ends(array, rng, least, largest):
    longest = array.shape.index(max(array.shape))
    spots = []
    for shift in (0, 1):
        where = [jax.random.randint(jax.random.fold_in(rng, axis), (), 0, length) for axis, length in enumerate(array.shape)]
        where[longest] = (where[longest] + shift) % array.shape[longest]
        spots.append(tuple(where))
    return array.at[spots[0]].set(least).at[spots[1]].set(largest)


def shard_levels(key, extent, pieces, smallest, high):
    gain = 1.0
    for dim, blocks in pieces:
        draws = jax.random.uniform(jax.random.fold_in(jax.random.fold_in(key, 6), dim), (blocks,), jnp.float32, smallest / len(pieces), high / len(pieces))
        gain = gain * jnp.repeat(jnp.exp(draws), extent[dim] // blocks).reshape((-1,) + (1,) * (len(extent) - 1 - dim))
    return gain


def scatter_about(rng, extent, deviation, reach, pieces=(), held_as=jnp.bfloat16):
    factor_of = shard_levels(rng, extent, pieces, -0.22, 0.18) if pieces else 1.0
    result = jax.random.normal(rng, extent, jnp.float32) * deviation * factor_of
    return jnp.minimum(jnp.maximum(result, -reach), reach).astype(held_as)


def setup_inputs(seed: int = 0) -> dict:
    streams_of = jax.random.split(jax.random.key(seed), 7)
    tokens = scatter_about(streams_of[0], (TOKENS, D), 1.0, 6.0, ((0, 32), (1, 8)))
    cotangent = scatter_about(streams_of[1], (TOKENS, D), 1.0, 6.0, ((0, 32), (1, 8)))
    gate_weight = scatter_about(streams_of[2], (D, FF), (D // 2) ** -0.5, 0.09375, ((0, 8), (1, 32)))
    up_weight = scatter_about(streams_of[3], (D, FF), (D // 2) ** -0.5, 0.09375, ((0, 8), (1, 32)))
    down_weight = scatter_about(streams_of[4], (FF, D), (FF // 2) ** -0.5, 0.046875, ((0, 32), (1, 8)))
    block_mask = set_ends((jax.random.randint(streams_of[5], (3, D // BLOCK, FF // BLOCK), 0, 2) < 1).astype(jnp.int32), jax.random.fold_in(streams_of[5], 1), 0, 1)
    return dict(tokens=tokens, cotangent=cotangent, gate_weight=gate_weight, up_weight=up_weight, down_weight=down_weight, block_mask=block_mask)


def masked(weight, mask):
    rows, cols = mask.shape
    shaped = weight.reshape(rows, weight.shape[0] // rows, cols, weight.shape[1] // cols)
    return (shaped * mask.astype(weight.dtype)[:, None, :, None]).reshape(weight.shape)


def grouped_sum(pairs, groups):
    width = pairs[0][0].shape[1] // groups
    first, weight0, wdim0 = pairs[0]
    outer = weight0.shape[1 - wdim0]

    def step(index, total):
        start = (index * width).astype(jnp.int32)
        part = jnp.zeros((first.shape[0], outer), jnp.float32)
        for left, weight, wdim in pairs:
            piece = lax.dynamic_slice_in_dim(left, start, width, 1)
            wpiece = lax.dynamic_slice_in_dim(weight, start, width, wdim)
            part = part + lax.dot_general(piece, wpiece, (((1,), (wdim,)), ((), ())), preferred_element_type=jnp.float32)
        rounded = lax.optimization_barrier(part.astype(jnp.bfloat16))
        return total + rounded.astype(jnp.float32)

    return lax.fori_loop(0, groups, step, jnp.zeros((first.shape[0], outer), jnp.float32))


def contract_rows(left, right):
    return lax.dot_general(left, right, (((0,), (0,)), ((), ())), preferred_element_type=jnp.float32)


def reference(tokens, cotangent, gate_weight, up_weight, down_weight, block_mask):
    masked_gate = masked(gate_weight, block_mask[0])
    masked_up = masked(up_weight, block_mask[1])
    masked_down = masked(down_weight, block_mask[2].T)
    gate = grouped_sum([(tokens, masked_gate, 0)], N_ROW)
    up = grouped_sum([(tokens, masked_up, 0)], N_ROW)
    sigma = jax.nn.sigmoid(gate)
    act = (gate * sigma * up).astype(jnp.bfloat16)
    layer_out = grouped_sum([(act, masked_down, 0)], N_COL).astype(jnp.bfloat16)
    dact = grouped_sum([(cotangent, masked_down, 1)], N_ROW)
    dgate = (dact * up * sigma * (1.0 + gate * (1.0 - sigma))).astype(jnp.bfloat16)
    dup = (dact * gate * sigma).astype(jnp.bfloat16)
    token_grad = grouped_sum([(dgate, masked_gate, 1), (dup, masked_up, 1)], N_COL).astype(jnp.bfloat16)
    scale = TOKENS ** -0.5
    gate_grad = masked(contract_rows(tokens, dgate) * scale, block_mask[0]).astype(jnp.bfloat16)
    up_grad = masked(contract_rows(tokens, dup) * scale, block_mask[1]).astype(jnp.bfloat16)
    down_grad = masked(contract_rows(act, cotangent) * scale, block_mask[2].T).astype(jnp.bfloat16)
    return (layer_out, token_grad, gate_grad, up_grad, down_grad)
```

```python
import jax
import jax.numpy as jnp
from jax import lax
from jax.sharding import PartitionSpec as P


def masked(weight, mask):
    rows, cols = mask.shape
    shaped = weight.reshape(rows, weight.shape[0] // rows, cols, weight.shape[1] // cols)
    return (shaped * mask.astype(weight.dtype)[:, None, :, None]).reshape(weight.shape)


def product(left, weight):
    return jnp.dot(left, weight, preferred_element_type=jnp.float32)


def product_t(left, weight):
    return lax.dot_general(
        left, weight, (((1,), (1,)), ((), ())), preferred_element_type=jnp.float32
    )


def contract_rows(left, right):
    return lax.dot_general(
        left, right, (((0,), (0,)), ((), ())), preferred_element_type=jnp.float32
    )


def gather_rows(local, axis, size):
    sent = jnp.broadcast_to(local[None], (size,) + local.shape)
    got = lax.all_to_all(sent, axis, 0, 0, tiled=False)
    return got.reshape((size * local.shape[0],) + local.shape[1:])


def reduce_rows(partial, axis, size):
    chunks = partial.astype(jnp.bfloat16).reshape((size, partial.shape[0] // size) + partial.shape[1:])
    got = lax.all_to_all(chunks, axis, 0, 0, tiled=False)
    return got.astype(jnp.float32).sum(axis=0)


def shards(tokens, cotangent, gate_weight, up_weight, down_weight, block_mask):
    n_row = lax.axis_size("row")
    n_col = lax.axis_size("col")
    masked_gate = masked(gate_weight, block_mask[0])
    masked_up = masked(up_weight, block_mask[1])
    masked_down = masked(down_weight, block_mask[2].T)
    feat = tokens.shape[1]
    both = gather_rows(jnp.concatenate([tokens, cotangent], axis=1), "col", n_col)
    panel = both[:, :feat]
    grad_panel = both[:, feat:]
    total_rows = panel.shape[0]
    width = masked_gate.shape[1]
    partials = jnp.concatenate(
        [
            product(panel, masked_gate).astype(jnp.bfloat16),
            product(panel, masked_up).astype(jnp.bfloat16),
            product_t(grad_panel, masked_down).astype(jnp.bfloat16),
        ],
        axis=1,
    )
    sums = reduce_rows(partials, "row", n_row)
    gate = sums[:, :width]
    up = sums[:, width : 2 * width]
    dact = sums[:, 2 * width :]
    sigma = jax.nn.sigmoid(gate)
    act = (gate * sigma * up).astype(jnp.bfloat16)
    dgate = (dact * up * sigma * (1.0 + gate * (1.0 - sigma))).astype(jnp.bfloat16)
    dup = (dact * gate * sigma).astype(jnp.bfloat16)
    full = lax.all_gather(jnp.concatenate([act, dgate, dup], axis=1), "row", axis=0, tiled=True)
    act_full = full[:, :width]
    dgate_full = full[:, width : 2 * width]
    dup_full = full[:, 2 * width :]
    out_partials = jnp.concatenate(
        [
            product(act_full, masked_down).astype(jnp.bfloat16),
            (product_t(dgate_full, masked_gate) + product_t(dup_full, masked_up)).astype(
                jnp.bfloat16
            ),
        ],
        axis=1,
    )
    outs = reduce_rows(out_partials, "col", n_col).astype(jnp.bfloat16)
    layer_out = outs[:, :feat]
    token_grad = outs[:, feat:]
    scale = total_rows ** (-0.5)
    gate_grad = masked(contract_rows(panel, dgate_full) * scale, block_mask[0]).astype(jnp.bfloat16)
    up_grad = masked(contract_rows(panel, dup_full) * scale, block_mask[1]).astype(jnp.bfloat16)
    down_grad = masked(contract_rows(act_full, grad_panel) * scale, block_mask[2].T).astype(
        jnp.bfloat16
    )
    return (layer_out, token_grad, gate_grad, up_grad, down_grad)


def solution(mesh):
    in_specs = (
        P("col", "row"),
        P("col", "row"),
        P("row", "col"),
        P("row", "col"),
        P("col", "row"),
        P(None, "row", "col"),
    )
    out_specs = (
        P("col", "row"),
        P("col", "row"),
        P("row", "col"),
        P("row", "col"),
        P("col", "row"),
    )
    return jax.shard_map(shards, mesh=mesh, in_specs=in_specs, out_specs=out_specs, check_vma=False)
```

```python
import jax
import jax.numpy as jnp
from jax import lax
from jax.sharding import PartitionSpec as P


def masked(weight, mask):
    rows, cols = mask.shape
    shaped = weight.reshape(rows, weight.shape[0] // rows, cols, weight.shape[1] // cols)
    return (shaped * mask.astype(weight.dtype)[:, None, :, None]).reshape(weight.shape)


def product(left, weight):
    return jnp.dot(left, weight, preferred_element_type=jnp.float32)


def product_t(left, weight):
    return lax.dot_general(
        left, weight, (((1,), (1,)), ((), ())), preferred_element_type=jnp.float32
    )


def contract_rows(left, right):
    return lax.dot_general(
        left, right, (((0,), (0,)), ((), ())), preferred_element_type=jnp.float32
    )


def gather_rows(local, axis, size):
    sent = jnp.broadcast_to(local[None], (size,) + local.shape)
    got = lax.all_to_all(sent, axis, 0, 0, tiled=False)
    return got.reshape((size * local.shape[0],) + local.shape[1:])


def reduce_rows(partial, axis, size):
    chunks = partial.astype(jnp.bfloat16).reshape((size, partial.shape[0] // size) + partial.shape[1:])
    got = lax.all_to_all(chunks, axis, 0, 0, tiled=False)
    return got.astype(jnp.float32).sum(axis=0)


def shards(tokens, cotangent, gate_weight, up_weight, down_weight, block_mask):
    n_row = lax.axis_size("row")
    n_col = lax.axis_size("col")
    masked_gate = masked(gate_weight, block_mask[0])
    masked_up = masked(up_weight, block_mask[1])
    masked_down = masked(down_weight, block_mask[2].T)
    feat = tokens.shape[1]
    panel = gather_rows(tokens, "col", n_col)
    grad_panel = gather_rows(cotangent, "col", n_col)
    total_rows = panel.shape[0]
    width = masked_gate.shape[1]
    fwd = reduce_rows(
        jnp.concatenate(
            [
                product(panel, masked_gate).astype(jnp.bfloat16),
                product(panel, masked_up).astype(jnp.bfloat16),
            ],
            axis=1,
        ),
        "row",
        n_row,
    )
    gate = fwd[:, :width]
    up = fwd[:, width:]
    sigma = jax.nn.sigmoid(gate)
    act = (gate * sigma * up).astype(jnp.bfloat16)
    act_full = lax.all_gather(act, "row", axis=0, tiled=True)
    layer_out = reduce_rows(product(act_full, masked_down), "col", n_col).astype(jnp.bfloat16)
    dact = reduce_rows(product_t(grad_panel, masked_down), "row", n_row)
    dgate = (dact * up * sigma * (1.0 + gate * (1.0 - sigma))).astype(jnp.bfloat16)
    dup = (dact * gate * sigma).astype(jnp.bfloat16)
    full = lax.all_gather(jnp.concatenate([dgate, dup], axis=1), "row", axis=0, tiled=True)
    dgate_full = full[:, :width]
    dup_full = full[:, width:]
    token_grad = reduce_rows(
        product_t(dgate_full, masked_gate) + product_t(dup_full, masked_up), "col", n_col
    ).astype(jnp.bfloat16)
    scale = total_rows ** (-0.5)
    gate_grad = masked(contract_rows(panel, dgate_full) * scale, block_mask[0]).astype(jnp.bfloat16)
    up_grad = masked(contract_rows(panel, dup_full) * scale, block_mask[1]).astype(jnp.bfloat16)
    down_grad = masked(contract_rows(act_full, grad_panel) * scale, block_mask[2].T).astype(
        jnp.bfloat16
    )
    return (layer_out, token_grad, gate_grad, up_grad, down_grad)


def solution(mesh):
    in_specs = (
        P("col", "row"),
        P("col", "row"),
        P("row", "col"),
        P("row", "col"),
        P("col", "row"),
        P(None, "row", "col"),
    )
    out_specs = (
        P("col", "row"),
        P("col", "row"),
        P("row", "col"),
        P("row", "col"),
        P("col", "row"),
    )
    return jax.shard_map(shards, mesh=mesh, in_specs=in_specs, out_specs=out_specs, check_vma=False)
```

```python
import jax
import jax.numpy as jnp
from jax import lax
from jax.sharding import Mesh
from jax.sharding import PartitionSpec as P

COL = ("y", "z")
ROW = ("x", "core")


def masked(weight, mask):
    rows, cols = mask.shape
    shaped = weight.reshape(rows, weight.shape[0] // rows, cols, weight.shape[1] // cols)
    return (shaped * mask.astype(weight.dtype)[:, None, :, None]).reshape(weight.shape)


def product(left, weight):
    return jnp.dot(left, weight, preferred_element_type=jnp.float32)


def product_t(left, weight):
    return lax.dot_general(
        left, weight, (((1,), (1,)), ((), ())), preferred_element_type=jnp.float32
    )


def contract_rows(left, right):
    return lax.dot_general(
        left, right, (((0,), (0,)), ((), ())), preferred_element_type=jnp.float32
    )


def gather_rows(local, axis):
    size = lax.axis_size(axis)
    sent = jnp.broadcast_to(local[None], (size,) + local.shape)
    got = lax.all_to_all(sent, axis, 0, 0, tiled=False)
    return got.reshape((size * local.shape[0],) + local.shape[1:])


def reduce_rows(partial, axis):
    size = lax.axis_size(axis)
    chunks = partial.astype(jnp.bfloat16).reshape((size, partial.shape[0] // size) + partial.shape[1:])
    got = lax.all_to_all(chunks, axis, 0, 0, tiled=False)
    return got.astype(jnp.float32).sum(axis=0)


def gather_col(local):
    return gather_rows(gather_rows(local, "z"), "y")


def reduce_col(partial):
    return reduce_rows(reduce_rows(partial, "y"), "z")


def reduce_row(partial):
    n_x = lax.axis_size("x")
    n_core = lax.axis_size("core")
    rows = partial.shape[0] // (n_x * n_core)
    split = partial.astype(jnp.bfloat16).reshape((n_x, n_core, rows) + partial.shape[1:])
    split = jnp.swapaxes(split, 0, 1)
    got = lax.all_to_all(split, "core", 0, 0, tiled=False).astype(jnp.float32).sum(axis=0)
    got = lax.all_to_all(got.astype(jnp.bfloat16), "x", 0, 0, tiled=False)
    return got.astype(jnp.float32).sum(axis=0)


def shards(tokens, cotangent, gate_weight, up_weight, down_weight, block_mask):
    masked_gate = masked(gate_weight, block_mask[0])
    masked_up = masked(up_weight, block_mask[1])
    masked_down = masked(down_weight, block_mask[2].T)
    feat = tokens.shape[1]
    both = gather_col(jnp.concatenate([tokens, cotangent], axis=1))
    panel = both[:, :feat]
    grad_panel = both[:, feat:]
    total_rows = panel.shape[0]
    width = masked_gate.shape[1]
    partials = jnp.concatenate(
        [
            product(panel, masked_gate).astype(jnp.bfloat16),
            product(panel, masked_up).astype(jnp.bfloat16),
            product_t(grad_panel, masked_down).astype(jnp.bfloat16),
        ],
        axis=1,
    )
    sums = reduce_row(partials)
    gate = sums[:, :width]
    up = sums[:, width : 2 * width]
    dact = sums[:, 2 * width :]
    sigma = jax.nn.sigmoid(gate)
    act = (gate * sigma * up).astype(jnp.bfloat16)
    dgate = (dact * up * sigma * (1.0 + gate * (1.0 - sigma))).astype(jnp.bfloat16)
    dup = (dact * gate * sigma).astype(jnp.bfloat16)
    full = lax.all_gather(jnp.concatenate([act, dgate, dup], axis=1), ROW, axis=0, tiled=True)
    act_full = full[:, :width]
    dgate_full = full[:, width : 2 * width]
    dup_full = full[:, 2 * width :]
    out_partials = jnp.concatenate(
        [
            product(act_full, masked_down).astype(jnp.bfloat16),
            (product_t(dgate_full, masked_gate) + product_t(dup_full, masked_up)).astype(
                jnp.bfloat16
            ),
        ],
        axis=1,
    )
    outs = reduce_col(out_partials).astype(jnp.bfloat16)
    layer_out = outs[:, :feat]
    token_grad = outs[:, feat:]
    scale = total_rows ** (-0.5)
    gate_grad = masked(contract_rows(panel, dgate_full) * scale, block_mask[0]).astype(jnp.bfloat16)
    up_grad = masked(contract_rows(panel, dup_full) * scale, block_mask[1]).astype(jnp.bfloat16)
    down_grad = masked(contract_rows(act_full, grad_panel) * scale, block_mask[2].T).astype(
        jnp.bfloat16
    )
    return (layer_out, token_grad, gate_grad, up_grad, down_grad)


def solution(mesh):
    n_row, n_col = mesh.devices.shape
    fine = Mesh(mesh.devices.reshape(n_row // 2, 2, 4, n_col // 4), ("x", "core", "y", "z"))
    in_specs = (
        P(COL, ROW),
        P(COL, ROW),
        P(ROW, COL),
        P(ROW, COL),
        P(COL, ROW),
        P(None, ROW, COL),
    )
    out_specs = (
        P(COL, ROW),
        P(COL, ROW),
        P(ROW, COL),
        P(ROW, COL),
        P(COL, ROW),
    )
    return jax.shard_map(shards, mesh=fine, in_specs=in_specs, out_specs=out_specs, check_vma=False)
```

```python
import jax
import jax.numpy as jnp
from jax import lax
from jax.sharding import Mesh
from jax.sharding import PartitionSpec as P

COL = ("y", "z")
ROW = ("x", "core")


def masked(weight, mask):
    rows, cols = mask.shape
    shaped = weight.reshape(rows, weight.shape[0] // rows, cols, weight.shape[1] // cols)
    return (shaped * mask.astype(weight.dtype)[:, None, :, None]).reshape(weight.shape)


def product(left, weight):
    return jnp.dot(left, weight, preferred_element_type=jnp.float32)


def product_t(left, weight):
    return lax.dot_general(
        left, weight, (((1,), (1,)), ((), ())), preferred_element_type=jnp.float32
    )


def contract_rows(left, right):
    return lax.dot_general(
        left, right, (((0,), (0,)), ((), ())), preferred_element_type=jnp.float32
    )


def gather_rows(local, axis):
    size = lax.axis_size(axis)
    sent = jnp.broadcast_to(local[None], (size,) + local.shape)
    got = lax.all_to_all(sent, axis, 0, 0, tiled=False)
    return got.reshape((size * local.shape[0],) + local.shape[1:])


def reduce_rows(partial, axis):
    size = lax.axis_size(axis)
    chunks = partial.astype(jnp.bfloat16).reshape((size, partial.shape[0] // size) + partial.shape[1:])
    got = lax.all_to_all(chunks, axis, 0, 0, tiled=False)
    return got.astype(jnp.float32).sum(axis=0)


def gather_col(local):
    return gather_rows(gather_rows(local, "z"), "y")


def reduce_col(partial):
    return reduce_rows(reduce_rows(partial, "y"), "z")


def reduce_row(partial):
    n_x = lax.axis_size("x")
    n_core = lax.axis_size("core")
    rows = partial.shape[0] // (n_x * n_core)
    split = partial.astype(jnp.bfloat16).reshape((n_x, n_core, rows) + partial.shape[1:])
    split = jnp.swapaxes(split, 0, 1)
    got = lax.all_to_all(split, "core", 0, 0, tiled=False).astype(jnp.float32).sum(axis=0)
    got = lax.all_to_all(got.astype(jnp.bfloat16), "x", 0, 0, tiled=False)
    return got.astype(jnp.float32).sum(axis=0)


def shards(tokens, cotangent, gate_weight, up_weight, down_weight, block_mask):
    masked_gate = masked(gate_weight, block_mask[0])
    masked_up = masked(up_weight, block_mask[1])
    masked_down = masked(down_weight, block_mask[2].T)
    feat = tokens.shape[1]
    both = gather_col(jnp.concatenate([tokens, cotangent], axis=1))
    panel = both[:, :feat]
    grad_panel = both[:, feat:]
    total_rows = panel.shape[0]
    width = masked_gate.shape[1]
    partials = jnp.concatenate(
        [
            product(panel, masked_gate).astype(jnp.bfloat16),
            product(panel, masked_up).astype(jnp.bfloat16),
            product_t(grad_panel, masked_down).astype(jnp.bfloat16),
        ],
        axis=1,
    )
    sums = reduce_row(partials)
    gate = sums[:, :width]
    up = sums[:, width : 2 * width]
    dact = sums[:, 2 * width :]
    sigma = jax.nn.sigmoid(gate)
    act = (gate * sigma * up).astype(jnp.bfloat16)
    dgate = (dact * up * sigma * (1.0 + gate * (1.0 - sigma))).astype(jnp.bfloat16)
    dup = (dact * gate * sigma).astype(jnp.bfloat16)
    full = gather_rows(jnp.concatenate([act, dgate, dup], axis=1), ROW)
    act_full = full[:, :width]
    dgate_full = full[:, width : 2 * width]
    dup_full = full[:, 2 * width :]
    out_partials = jnp.concatenate(
        [
            product(act_full, masked_down).astype(jnp.bfloat16),
            (product_t(dgate_full, masked_gate) + product_t(dup_full, masked_up)).astype(
                jnp.bfloat16
            ),
        ],
        axis=1,
    )
    outs = reduce_col(out_partials).astype(jnp.bfloat16)
    layer_out = outs[:, :feat]
    token_grad = outs[:, feat:]
    scale = total_rows ** (-0.5)
    gate_grad = masked(contract_rows(panel, dgate_full) * scale, block_mask[0]).astype(jnp.bfloat16)
    up_grad = masked(contract_rows(panel, dup_full) * scale, block_mask[1]).astype(jnp.bfloat16)
    down_grad = masked(contract_rows(act_full, grad_panel) * scale, block_mask[2].T).astype(
        jnp.bfloat16
    )
    return (layer_out, token_grad, gate_grad, up_grad, down_grad)


def solution(mesh):
    n_row, n_col = mesh.devices.shape
    fine = Mesh(mesh.devices.reshape(n_row // 2, 2, 4, n_col // 4), ("x", "core", "y", "z"))
    in_specs = (
        P(COL, ROW),
        P(COL, ROW),
        P(ROW, COL),
        P(ROW, COL),
        P(COL, ROW),
        P(None, ROW, COL),
    )
    out_specs = (
        P(COL, ROW),
        P(COL, ROW),
        P(ROW, COL),
        P(ROW, COL),
        P(COL, ROW),
    )
    return jax.shard_map(shards, mesh=fine, in_specs=in_specs, out_specs=out_specs, check_vma=False)
```

```python
import jax
import jax.numpy as jnp
from jax import lax
from jax.sharding import Mesh
from jax.sharding import PartitionSpec as P

COL = ("y", "z")
ROW = ("x", "core")


def masked(weight, mask):
    rows, cols = mask.shape
    shaped = weight.reshape(rows, weight.shape[0] // rows, cols, weight.shape[1] // cols)
    return (shaped * mask.astype(weight.dtype)[:, None, :, None]).reshape(weight.shape)


def product(left, weight):
    return jnp.dot(left, weight, preferred_element_type=jnp.float32)


def product_t(left, weight):
    return lax.dot_general(
        left, weight, (((1,), (1,)), ((), ())), preferred_element_type=jnp.float32
    )


def contract_rows(left, right):
    return lax.dot_general(
        left, right, (((0,), (0,)), ((), ())), preferred_element_type=jnp.float32
    )


def gather_rows(local, axis):
    size = lax.axis_size(axis)
    sent = jnp.broadcast_to(local[None], (size,) + local.shape)
    got = lax.all_to_all(sent, axis, 0, 0, tiled=False)
    return got.reshape((size * local.shape[0],) + local.shape[1:])


def reduce_rows(partial, axis):
    size = lax.axis_size(axis)
    chunks = partial.astype(jnp.bfloat16).reshape((size, partial.shape[0] // size) + partial.shape[1:])
    got = lax.all_to_all(chunks, axis, 0, 0, tiled=False)
    return got.astype(jnp.float32).sum(axis=0)


def gather_col(local):
    return gather_rows(gather_rows(local, "z"), "y")


def reduce_col(partial):
    return reduce_rows(reduce_rows(partial, "y"), "z")


def reduce_row(partial):
    n_x = lax.axis_size("x")
    n_core = lax.axis_size("core")
    rows = partial.shape[0] // (n_x * n_core)
    split = partial.astype(jnp.bfloat16).reshape((n_x, n_core, rows) + partial.shape[1:])
    split = jnp.swapaxes(split, 0, 1)
    got = lax.all_to_all(split, "core", 0, 0, tiled=False).astype(jnp.float32).sum(axis=0)
    got = lax.all_to_all(got.astype(jnp.bfloat16), "x", 0, 0, tiled=False)
    return got.astype(jnp.float32).sum(axis=0)


def gather_row(local):
    n_x = lax.axis_size("x")
    n_core = lax.axis_size("core")
    over_x = gather_rows(local, "x").reshape((n_x,) + local.shape)
    sent = jnp.broadcast_to(over_x[None], (n_core,) + over_x.shape)
    both = lax.all_to_all(sent, "core", 0, 0, tiled=False)
    return jnp.swapaxes(both, 0, 1).reshape((n_x * n_core * local.shape[0],) + local.shape[1:])


def shards(tokens, cotangent, gate_weight, up_weight, down_weight, block_mask):
    masked_gate = masked(gate_weight, block_mask[0])
    masked_up = masked(up_weight, block_mask[1])
    masked_down = masked(down_weight, block_mask[2].T)
    feat = tokens.shape[1]
    both = gather_col(jnp.concatenate([tokens, cotangent], axis=1))
    panel = both[:, :feat]
    grad_panel = both[:, feat:]
    total_rows = panel.shape[0]
    width = masked_gate.shape[1]
    partials = jnp.concatenate(
        [
            product(panel, masked_gate).astype(jnp.bfloat16),
            product(panel, masked_up).astype(jnp.bfloat16),
            product_t(grad_panel, masked_down).astype(jnp.bfloat16),
        ],
        axis=1,
    )
    sums = reduce_row(partials)
    gate = sums[:, :width]
    up = sums[:, width : 2 * width]
    dact = sums[:, 2 * width :]
    sigma = jax.nn.sigmoid(gate)
    act = (gate * sigma * up).astype(jnp.bfloat16)
    dgate = (dact * up * sigma * (1.0 + gate * (1.0 - sigma))).astype(jnp.bfloat16)
    dup = (dact * gate * sigma).astype(jnp.bfloat16)
    full = gather_row(jnp.concatenate([act, dgate, dup], axis=1))
    act_full = full[:, :width]
    dgate_full = full[:, width : 2 * width]
    dup_full = full[:, 2 * width :]
    out_partials = jnp.concatenate(
        [
            product(act_full, masked_down).astype(jnp.bfloat16),
            (product_t(dgate_full, masked_gate) + product_t(dup_full, masked_up)).astype(
                jnp.bfloat16
            ),
        ],
        axis=1,
    )
    outs = reduce_col(out_partials).astype(jnp.bfloat16)
    layer_out = outs[:, :feat]
    token_grad = outs[:, feat:]
    scale = total_rows ** (-0.5)
    gate_grad = masked(contract_rows(panel, dgate_full) * scale, block_mask[0]).astype(jnp.bfloat16)
    up_grad = masked(contract_rows(panel, dup_full) * scale, block_mask[1]).astype(jnp.bfloat16)
    down_grad = masked(contract_rows(act_full, grad_panel) * scale, block_mask[2].T).astype(
        jnp.bfloat16
    )
    return (layer_out, token_grad, gate_grad, up_grad, down_grad)


def solution(mesh):
    n_row, n_col = mesh.devices.shape
    fine = Mesh(mesh.devices.reshape(n_row // 2, 2, 4, n_col // 4), ("x", "core", "y", "z"))
    in_specs = (
        P(COL, ROW),
        P(COL, ROW),
        P(ROW, COL),
        P(ROW, COL),
        P(COL, ROW),
        P(None, ROW, COL),
    )
    out_specs = (
        P(COL, ROW),
        P(COL, ROW),
        P(ROW, COL),
        P(ROW, COL),
        P(COL, ROW),
    )
    return jax.shard_map(shards, mesh=fine, in_specs=in_specs, out_specs=out_specs, check_vma=False)
```

```python
import jax
import jax.numpy as jnp
from jax import lax
from jax.sharding import Mesh
from jax.sharding import PartitionSpec as P

COL = ("y", "z")
ROW = ("x", "core")


def masked(weight, mask):
    rows, cols = mask.shape
    shaped = weight.reshape(rows, weight.shape[0] // rows, cols, weight.shape[1] // cols)
    return (shaped * mask.astype(weight.dtype)[:, None, :, None]).reshape(weight.shape)


def product(left, weight):
    return jnp.dot(left, weight, preferred_element_type=jnp.float32)


def product_t(left, weight):
    return lax.dot_general(
        left, weight, (((1,), (1,)), ((), ())), preferred_element_type=jnp.float32
    )


def contract_rows(left, right):
    return lax.dot_general(
        left, right, (((0,), (0,)), ((), ())), preferred_element_type=jnp.float32
    )


def add_blocks(got):
    total = got[0].astype(jnp.float32)
    for i in range(1, got.shape[0]):
        total = total + got[i].astype(jnp.float32)
    return total


def gather_rows(local, axis):
    size = lax.axis_size(axis)
    sent = jnp.broadcast_to(local[None], (size,) + local.shape)
    got = lax.all_to_all(sent, axis, 0, 0, tiled=False)
    return got.reshape((size * local.shape[0],) + local.shape[1:])


def reduce_rows(partial, axis):
    size = lax.axis_size(axis)
    chunks = partial.astype(jnp.bfloat16).reshape((size, partial.shape[0] // size) + partial.shape[1:])
    got = lax.all_to_all(chunks, axis, 0, 0, tiled=False)
    return add_blocks(got)


def gather_col(local):
    return gather_rows(gather_rows(local, "z"), "y")


def reduce_col(partial):
    return reduce_rows(reduce_rows(partial, "y"), "z")


def reduce_row(partial):
    n_x = lax.axis_size("x")
    n_core = lax.axis_size("core")
    rows = partial.shape[0] // (n_x * n_core)
    split = partial.astype(jnp.bfloat16).reshape((n_x, n_core, rows) + partial.shape[1:])
    split = jnp.swapaxes(split, 0, 1)
    got = add_blocks(lax.all_to_all(split, "core", 0, 0, tiled=False))
    return add_blocks(lax.all_to_all(got.astype(jnp.bfloat16), "x", 0, 0, tiled=False))


def gather_row(local):
    n_x = lax.axis_size("x")
    n_core = lax.axis_size("core")
    over_x = gather_rows(local, "x").reshape((n_x,) + local.shape)
    sent = jnp.broadcast_to(over_x[None], (n_core,) + over_x.shape)
    both = lax.all_to_all(sent, "core", 0, 0, tiled=False)
    return jnp.swapaxes(both, 0, 1).reshape((n_x * n_core * local.shape[0],) + local.shape[1:])


def shards(tokens, cotangent, gate_weight, up_weight, down_weight, block_mask):
    masked_gate = masked(gate_weight, block_mask[0])
    masked_up = masked(up_weight, block_mask[1])
    masked_down = masked(down_weight, block_mask[2].T)
    feat = tokens.shape[1]
    both = gather_col(jnp.concatenate([tokens, cotangent], axis=1))
    panel = both[:, :feat]
    grad_panel = both[:, feat:]
    total_rows = panel.shape[0]
    width = masked_gate.shape[1]
    partials = jnp.concatenate(
        [
            product(panel, masked_gate).astype(jnp.bfloat16),
            product(panel, masked_up).astype(jnp.bfloat16),
            product_t(grad_panel, masked_down).astype(jnp.bfloat16),
        ],
        axis=1,
    )
    sums = reduce_row(partials)
    gate = sums[:, :width]
    up = sums[:, width : 2 * width]
    dact = sums[:, 2 * width :]
    sigma = jax.nn.sigmoid(gate)
    act = (gate * sigma * up).astype(jnp.bfloat16)
    dgate = (dact * up * sigma * (1.0 + gate * (1.0 - sigma))).astype(jnp.bfloat16)
    dup = (dact * gate * sigma).astype(jnp.bfloat16)
    full = gather_row(jnp.concatenate([act, dgate, dup], axis=1))
    act_full = full[:, :width]
    dgate_full = full[:, width : 2 * width]
    dup_full = full[:, 2 * width :]
    out_partials = jnp.concatenate(
        [
            product(act_full, masked_down).astype(jnp.bfloat16),
            (product_t(dgate_full, masked_gate) + product_t(dup_full, masked_up)).astype(
                jnp.bfloat16
            ),
        ],
        axis=1,
    )
    outs = reduce_col(out_partials).astype(jnp.bfloat16)
    layer_out = outs[:, :feat]
    token_grad = outs[:, feat:]
    scale = total_rows ** (-0.5)
    gate_grad = masked(contract_rows(panel, dgate_full) * scale, block_mask[0]).astype(jnp.bfloat16)
    up_grad = masked(contract_rows(panel, dup_full) * scale, block_mask[1]).astype(jnp.bfloat16)
    down_grad = masked(contract_rows(act_full, grad_panel) * scale, block_mask[2].T).astype(
        jnp.bfloat16
    )
    return (layer_out, token_grad, gate_grad, up_grad, down_grad)


def solution(mesh):
    n_row, n_col = mesh.devices.shape
    fine = Mesh(mesh.devices.reshape(n_row // 2, 2, 4, n_col // 4), ("x", "core", "y", "z"))
    in_specs = (
        P(COL, ROW),
        P(COL, ROW),
        P(ROW, COL),
        P(ROW, COL),
        P(COL, ROW),
        P(None, ROW, COL),
    )
    out_specs = (
        P(COL, ROW),
        P(COL, ROW),
        P(ROW, COL),
        P(ROW, COL),
        P(COL, ROW),
    )
    return jax.shard_map(shards, mesh=fine, in_specs=in_specs, out_specs=out_specs, check_vma=False)
```

```python
import jax
import jax.numpy as jnp
from jax import lax
from jax.sharding import Mesh
from jax.sharding import PartitionSpec as P

COL = ("y", "z")
ROW = ("x", "core")


def masked(weight, mask):
    rows, cols = mask.shape
    shaped = weight.reshape(rows, weight.shape[0] // rows, cols, weight.shape[1] // cols)
    return (shaped * mask.astype(weight.dtype)[:, None, :, None]).reshape(weight.shape)


def product(left, weight):
    return jnp.dot(left, weight, preferred_element_type=jnp.float32)


def product_t(left, weight):
    return lax.dot_general(
        left, weight, (((1,), (1,)), ((), ())), preferred_element_type=jnp.float32
    )


def contract_rows(left, right):
    return lax.dot_general(
        left, right, (((0,), (0,)), ((), ())), preferred_element_type=jnp.float32
    )


def add_blocks(got):
    total = got[0].astype(jnp.float32)
    for i in range(1, got.shape[0]):
        total = total + got[i].astype(jnp.float32)
    return total


def gather_rows(local, axis):
    size = lax.axis_size(axis)
    sent = jnp.broadcast_to(local[None], (size,) + local.shape)
    got = lax.all_to_all(sent, axis, 0, 0, tiled=False)
    return got.reshape((size * local.shape[0],) + local.shape[1:])


def reduce_rows(partial, axis):
    size = lax.axis_size(axis)
    chunks = partial.astype(jnp.bfloat16).reshape((size, partial.shape[0] // size) + partial.shape[1:])
    got = lax.all_to_all(chunks, axis, 0, 0, tiled=False)
    return add_blocks(got)


def gather_col(local):
    return gather_rows(gather_rows(local, "z"), "y")


def reduce_col(partial):
    return reduce_rows(reduce_rows(partial, "y"), "z")


def reduce_row(partial):
    n_x = lax.axis_size("x")
    n_core = lax.axis_size("core")
    rows = partial.shape[0] // (n_x * n_core)
    split = partial.astype(jnp.bfloat16).reshape((n_core, n_x, rows) + partial.shape[1:])
    got = add_blocks(lax.all_to_all(split, "core", 0, 0, tiled=False))
    return add_blocks(lax.all_to_all(got.astype(jnp.bfloat16), "x", 0, 0, tiled=False))


def gather_row(local):
    n_x = lax.axis_size("x")
    n_core = lax.axis_size("core")
    over_x = gather_rows(local, "x").reshape((n_x,) + local.shape)
    sent = jnp.broadcast_to(over_x[None], (n_core,) + over_x.shape)
    both = lax.all_to_all(sent, "core", 0, 0, tiled=False)
    return both.reshape((n_core * n_x * local.shape[0],) + local.shape[1:])


def shards(tokens, cotangent, gate_weight, up_weight, down_weight, block_mask):
    masked_gate = masked(gate_weight, block_mask[0])
    masked_up = masked(up_weight, block_mask[1])
    masked_down = masked(down_weight, block_mask[2].T)
    feat = tokens.shape[1]
    both = gather_col(jnp.concatenate([tokens, cotangent], axis=1))
    panel = both[:, :feat]
    grad_panel = both[:, feat:]
    total_rows = panel.shape[0]
    width = masked_gate.shape[1]
    partials = jnp.concatenate(
        [
            product(panel, masked_gate).astype(jnp.bfloat16),
            product(panel, masked_up).astype(jnp.bfloat16),
            product_t(grad_panel, masked_down).astype(jnp.bfloat16),
        ],
        axis=1,
    )
    sums = reduce_row(partials)
    gate = sums[:, :width]
    up = sums[:, width : 2 * width]
    dact = sums[:, 2 * width :]
    sigma = jax.nn.sigmoid(gate)
    act = (gate * sigma * up).astype(jnp.bfloat16)
    dgate = (dact * up * sigma * (1.0 + gate * (1.0 - sigma))).astype(jnp.bfloat16)
    dup = (dact * gate * sigma).astype(jnp.bfloat16)
    full = gather_row(jnp.concatenate([act, dgate, dup], axis=1))
    act_full = full[:, :width]
    dgate_full = full[:, width : 2 * width]
    dup_full = full[:, 2 * width :]
    out_partials = jnp.concatenate(
        [
            product(act_full, masked_down).astype(jnp.bfloat16),
            (product_t(dgate_full, masked_gate) + product_t(dup_full, masked_up)).astype(
                jnp.bfloat16
            ),
        ],
        axis=1,
    )
    outs = reduce_col(out_partials).astype(jnp.bfloat16)
    layer_out = outs[:, :feat]
    token_grad = outs[:, feat:]
    scale = total_rows ** (-0.5)
    gate_grad = masked(contract_rows(panel, dgate_full) * scale, block_mask[0]).astype(jnp.bfloat16)
    up_grad = masked(contract_rows(panel, dup_full) * scale, block_mask[1]).astype(jnp.bfloat16)
    down_grad = masked(contract_rows(act_full, grad_panel) * scale, block_mask[2].T).astype(
        jnp.bfloat16
    )
    return (layer_out, token_grad, gate_grad, up_grad, down_grad)


def solution(mesh):
    n_row, n_col = mesh.devices.shape
    fine = Mesh(mesh.devices.reshape(n_row // 2, 2, 4, n_col // 4), ("x", "core", "y", "z"))
    in_specs = (
        P(COL, ROW),
        P(COL, ROW),
        P(ROW, COL),
        P(ROW, COL),
        P(COL, ROW),
        P(None, ROW, COL),
    )
    out_specs = (
        P(COL, ROW),
        P(COL, ROW),
        P(ROW, COL),
        P(ROW, COL),
        P(COL, ROW),
    )
    return jax.shard_map(shards, mesh=fine, in_specs=in_specs, out_specs=out_specs, check_vma=False)
```

```python
import jax
import jax.numpy as jnp
from jax import lax
from jax.sharding import Mesh
from jax.sharding import PartitionSpec as P

COL = ("y", "z")
ROW = ("x", "core")


def masked(weight, mask):
    rows, cols = mask.shape
    shaped = weight.reshape(rows, weight.shape[0] // rows, cols, weight.shape[1] // cols)
    return (shaped * mask.astype(weight.dtype)[:, None, :, None]).reshape(weight.shape)


def product(left, weight):
    return jnp.dot(left, weight, preferred_element_type=jnp.float32)


def product_t(left, weight):
    return lax.dot_general(
        left, weight, (((1,), (1,)), ((), ())), preferred_element_type=jnp.float32
    )


def contract_rows(left, right):
    return lax.dot_general(
        left, right, (((0,), (0,)), ((), ())), preferred_element_type=jnp.float32
    )


def add_blocks(got):
    total = got[0].astype(jnp.float32)
    for i in range(1, got.shape[0]):
        total = total + got[i].astype(jnp.float32)
    return total


def gather_rows(local, axis):
    size = lax.axis_size(axis)
    sent = jnp.broadcast_to(local[None], (size,) + local.shape)
    got = lax.all_to_all(sent, axis, 0, 0, tiled=False)
    return got.reshape((size * local.shape[0],) + local.shape[1:])


def reduce_rows(partial, axis):
    size = lax.axis_size(axis)
    chunks = partial.astype(jnp.bfloat16).reshape((size, partial.shape[0] // size) + partial.shape[1:])
    got = lax.all_to_all(chunks, axis, 0, 0, tiled=False)
    return add_blocks(got)


def gather_col(local):
    return gather_rows(gather_rows(local, "z"), "y")


def reduce_col(partial):
    return reduce_rows(reduce_rows(partial, "y"), "z")


def swap_core(value):
    return lax.ppermute(value, "core", [(0, 1), (1, 0)])


def reduce_row(partial):
    n_x = lax.axis_size("x")
    n_core = lax.axis_size("core")
    rows = partial.shape[0] // (n_x * n_core)
    split = partial.astype(jnp.bfloat16).reshape((n_core, n_x, rows) + partial.shape[1:])
    me = lax.axis_index("core")
    mine = lax.dynamic_index_in_dim(split, me, 0, keepdims=False)
    other = lax.dynamic_index_in_dim(split, 1 - me, 0, keepdims=False)
    got = mine.astype(jnp.float32) + swap_core(other).astype(jnp.float32)
    return add_blocks(lax.all_to_all(got.astype(jnp.bfloat16), "x", 0, 0, tiled=False))


def gather_row(local):
    over_x = gather_rows(local, "x")
    theirs = swap_core(over_x)
    first = lax.axis_index("core") == 0
    both = jnp.concatenate([jnp.where(first, over_x, theirs), jnp.where(first, theirs, over_x)], axis=0)
    return both


def shards(tokens, cotangent, gate_weight, up_weight, down_weight, block_mask):
    masked_gate = masked(gate_weight, block_mask[0])
    masked_up = masked(up_weight, block_mask[1])
    masked_down = masked(down_weight, block_mask[2].T)
    feat = tokens.shape[1]
    both = gather_col(jnp.concatenate([tokens, cotangent], axis=1))
    panel = both[:, :feat]
    grad_panel = both[:, feat:]
    total_rows = panel.shape[0]
    width = masked_gate.shape[1]
    partials = jnp.concatenate(
        [
            product(panel, masked_gate).astype(jnp.bfloat16),
            product(panel, masked_up).astype(jnp.bfloat16),
            product_t(grad_panel, masked_down).astype(jnp.bfloat16),
        ],
        axis=1,
    )
    sums = reduce_row(partials)
    gate = sums[:, :width]
    up = sums[:, width : 2 * width]
    dact = sums[:, 2 * width :]
    sigma = jax.nn.sigmoid(gate)
    act = (gate * sigma * up).astype(jnp.bfloat16)
    dgate = (dact * up * sigma * (1.0 + gate * (1.0 - sigma))).astype(jnp.bfloat16)
    dup = (dact * gate * sigma).astype(jnp.bfloat16)
    full = gather_row(jnp.concatenate([act, dgate, dup], axis=1))
    act_full = full[:, :width]
    dgate_full = full[:, width : 2 * width]
    dup_full = full[:, 2 * width :]
    out_partials = jnp.concatenate(
        [
            product(act_full, masked_down).astype(jnp.bfloat16),
            (product_t(dgate_full, masked_gate) + product_t(dup_full, masked_up)).astype(
                jnp.bfloat16
            ),
        ],
        axis=1,
    )
    outs = reduce_col(out_partials).astype(jnp.bfloat16)
    layer_out = outs[:, :feat]
    token_grad = outs[:, feat:]
    scale = total_rows ** (-0.5)
    gate_grad = masked(contract_rows(panel, dgate_full) * scale, block_mask[0]).astype(jnp.bfloat16)
    up_grad = masked(contract_rows(panel, dup_full) * scale, block_mask[1]).astype(jnp.bfloat16)
    down_grad = masked(contract_rows(act_full, grad_panel) * scale, block_mask[2].T).astype(
        jnp.bfloat16
    )
    return (layer_out, token_grad, gate_grad, up_grad, down_grad)


def solution(mesh):
    n_row, n_col = mesh.devices.shape
    fine = Mesh(mesh.devices.reshape(n_row // 2, 2, 4, n_col // 4), ("x", "core", "y", "z"))
    in_specs = (
        P(COL, ROW),
        P(COL, ROW),
        P(ROW, COL),
        P(ROW, COL),
        P(COL, ROW),
        P(None, ROW, COL),
    )
    out_specs = (
        P(COL, ROW),
        P(COL, ROW),
        P(ROW, COL),
        P(ROW, COL),
        P(COL, ROW),
    )
    return jax.shard_map(shards, mesh=fine, in_specs=in_specs, out_specs=out_specs, check_vma=False)
```

```python
import jax
import jax.numpy as jnp
from jax import lax
from jax.sharding import Mesh
from jax.sharding import PartitionSpec as P

COL = ("y", "z")
ROW = ("x", "core")


def masked(weight, mask):
    rows, cols = mask.shape
    shaped = weight.reshape(rows, weight.shape[0] // rows, cols, weight.shape[1] // cols)
    return (shaped * mask.astype(weight.dtype)[:, None, :, None]).reshape(weight.shape)


def product(left, weight):
    return jnp.dot(left, weight, preferred_element_type=jnp.float32)


def product_t(left, weight):
    return lax.dot_general(
        left, weight, (((1,), (1,)), ((), ())), preferred_element_type=jnp.float32
    )


def contract_rows(left, right):
    return lax.dot_general(
        left, right, (((0,), (0,)), ((), ())), preferred_element_type=jnp.float32
    )


def add_blocks(got):
    total = got[0].astype(jnp.float32)
    for i in range(1, got.shape[0]):
        total = total + got[i].astype(jnp.float32)
    return total


def gather_rows(local, axis):
    size = lax.axis_size(axis)
    sent = jnp.broadcast_to(local[None], (size,) + local.shape)
    got = lax.all_to_all(sent, axis, 0, 0, tiled=False)
    return got.reshape((size * local.shape[0],) + local.shape[1:])


def reduce_rows(partial, axis):
    size = lax.axis_size(axis)
    chunks = partial.astype(jnp.bfloat16).reshape((size, partial.shape[0] // size) + partial.shape[1:])
    got = lax.all_to_all(chunks, axis, 0, 0, tiled=False)
    return add_blocks(got)


def gather_col(local):
    return gather_rows(gather_rows(local, "z"), "y")


def reduce_col(partial):
    return reduce_rows(reduce_rows(partial, "y"), "z")


def reduce_row(partial):
    n_x = lax.axis_size("x")
    n_core = lax.axis_size("core")
    rows = partial.shape[0] // (n_x * n_core)
    split = partial.astype(jnp.bfloat16).reshape((n_core, n_x, rows) + partial.shape[1:])
    got = add_blocks(lax.all_to_all(split, "core", 0, 0, tiled=False))
    return add_blocks(lax.all_to_all(got.astype(jnp.bfloat16), "x", 0, 0, tiled=False))


def gather_row(local):
    n_x = lax.axis_size("x")
    n_core = lax.axis_size("core")
    over_x = gather_rows(local, "x").reshape((n_x,) + local.shape)
    sent = jnp.broadcast_to(over_x[None], (n_core,) + over_x.shape)
    both = lax.all_to_all(sent, "core", 0, 0, tiled=False)
    return both.reshape((n_core * n_x * local.shape[0],) + local.shape[1:])


def shards(tokens, cotangent, gate_weight, up_weight, down_weight, block_mask):
    masked_gate = masked(gate_weight, block_mask[0])
    masked_up = masked(up_weight, block_mask[1])
    masked_down = masked(down_weight, block_mask[2].T)
    feat = tokens.shape[1]
    both = gather_col(jnp.concatenate([tokens, cotangent], axis=1))
    panel = both[:, :feat]
    grad_panel = both[:, feat:]
    total_rows = panel.shape[0]
    width = masked_gate.shape[1]
    partials = jnp.concatenate(
        [
            product(panel, masked_gate).astype(jnp.bfloat16),
            product(panel, masked_up).astype(jnp.bfloat16),
            product_t(grad_panel, masked_down).astype(jnp.bfloat16),
        ],
        axis=1,
    )
    sums = reduce_row(partials)
    gate = sums[:, :width]
    up = sums[:, width : 2 * width]
    dact = sums[:, 2 * width :]
    sigma = jax.nn.sigmoid(gate)
    act = (gate * sigma * up).astype(jnp.bfloat16)
    dgate = (dact * up * sigma * (1.0 + gate * (1.0 - sigma))).astype(jnp.bfloat16)
    dup = (dact * gate * sigma).astype(jnp.bfloat16)
    full = gather_row(jnp.concatenate([act, dgate, dup], axis=1))
    act_full = full[:, :width]
    dgate_full = full[:, width : 2 * width]
    dup_full = full[:, 2 * width :]
    out_partials = jnp.concatenate(
        [
            product(act_full, masked_down).astype(jnp.bfloat16),
            product_t(full[:, width:], jnp.concatenate([masked_gate, masked_up], axis=1)).astype(
                jnp.bfloat16
            ),
        ],
        axis=1,
    )
    outs = reduce_col(out_partials).astype(jnp.bfloat16)
    layer_out = outs[:, :feat]
    token_grad = outs[:, feat:]
    scale = total_rows ** (-0.5)
    gate_grad = masked(contract_rows(panel, dgate_full) * scale, block_mask[0]).astype(jnp.bfloat16)
    up_grad = masked(contract_rows(panel, dup_full) * scale, block_mask[1]).astype(jnp.bfloat16)
    down_grad = masked(contract_rows(act_full, grad_panel) * scale, block_mask[2].T).astype(
        jnp.bfloat16
    )
    return (layer_out, token_grad, gate_grad, up_grad, down_grad)


def solution(mesh):
    n_row, n_col = mesh.devices.shape
    fine = Mesh(mesh.devices.reshape(n_row // 2, 2, 4, n_col // 4), ("x", "core", "y", "z"))
    in_specs = (
        P(COL, ROW),
        P(COL, ROW),
        P(ROW, COL),
        P(ROW, COL),
        P(COL, ROW),
        P(None, ROW, COL),
    )
    out_specs = (
        P(COL, ROW),
        P(COL, ROW),
        P(ROW, COL),
        P(ROW, COL),
        P(COL, ROW),
    )
    return jax.shard_map(shards, mesh=fine, in_specs=in_specs, out_specs=out_specs, check_vma=False)
```

```python
import jax
import jax.numpy as jnp
from jax import lax
from jax.sharding import Mesh
from jax.sharding import PartitionSpec as P

COL = ("y", "z")
ROW = ("x", "core")


def masked(weight, mask):
    rows, cols = mask.shape
    shaped = weight.reshape(rows, weight.shape[0] // rows, cols, weight.shape[1] // cols)
    return (shaped * mask.astype(weight.dtype)[:, None, :, None]).reshape(weight.shape)


def product(left, weight):
    return jnp.dot(left, weight, preferred_element_type=jnp.float32)


def product_t(left, weight):
    return lax.dot_general(
        left, weight, (((1,), (1,)), ((), ())), preferred_element_type=jnp.float32
    )


def contract_rows(left, right):
    return lax.dot_general(
        left, right, (((0,), (0,)), ((), ())), preferred_element_type=jnp.float32
    )


def add_blocks(got):
    total = got[0].astype(jnp.float32)
    for i in range(1, got.shape[0]):
        total = total + got[i].astype(jnp.float32)
    return total


def gather_rows(local, axis):
    size = lax.axis_size(axis)
    sent = jnp.broadcast_to(local[None], (size,) + local.shape)
    got = lax.all_to_all(sent, axis, 0, 0, tiled=False)
    return got.reshape((size * local.shape[0],) + local.shape[1:])


def reduce_rows(partial, axis):
    size = lax.axis_size(axis)
    chunks = partial.astype(jnp.bfloat16).reshape((size, partial.shape[0] // size) + partial.shape[1:])
    got = lax.all_to_all(chunks, axis, 0, 0, tiled=False)
    return add_blocks(got)


def gather_col(local):
    return gather_rows(gather_rows(local, "z"), "y")


def reduce_col(partial):
    return reduce_rows(reduce_rows(partial, "y"), "z")


def reduce_row(partial):
    n_x = lax.axis_size("x")
    n_core = lax.axis_size("core")
    rows = partial.shape[0] // (n_x * n_core)
    split = partial.astype(jnp.bfloat16).reshape((n_core, n_x, rows) + partial.shape[1:])
    got = add_blocks(lax.all_to_all(split, "core", 0, 0, tiled=False))
    return add_blocks(lax.all_to_all(got.astype(jnp.bfloat16), "x", 0, 0, tiled=False))


def gather_row(local):
    n_x = lax.axis_size("x")
    n_core = lax.axis_size("core")
    over_x = gather_rows(local, "x").reshape((n_x,) + local.shape)
    sent = jnp.broadcast_to(over_x[None], (n_core,) + over_x.shape)
    both = lax.all_to_all(sent, "core", 0, 0, tiled=False)
    return both.reshape((n_core * n_x * local.shape[0],) + local.shape[1:])


def shards(tokens, cotangent, gate_weight, up_weight, down_weight, block_mask):
    masked_gate = masked(gate_weight, block_mask[0])
    masked_up = masked(up_weight, block_mask[1])
    masked_down = masked(down_weight, block_mask[2].T)
    gate_up = jnp.concatenate([masked_gate, masked_up], axis=1)
    feat = tokens.shape[1]
    both = gather_col(jnp.concatenate([tokens, cotangent], axis=1))
    panel = both[:, :feat]
    grad_panel = both[:, feat:]
    total_rows = panel.shape[0]
    width = masked_gate.shape[1]
    partials = jnp.concatenate(
        [
            product(panel, gate_up).astype(jnp.bfloat16),
            product_t(grad_panel, masked_down).astype(jnp.bfloat16),
        ],
        axis=1,
    )
    sums = reduce_row(partials)
    gate = sums[:, :width]
    up = sums[:, width : 2 * width]
    dact = sums[:, 2 * width :]
    sigma = jax.nn.sigmoid(gate)
    act = (gate * sigma * up).astype(jnp.bfloat16)
    dgate = (dact * up * sigma * (1.0 + gate * (1.0 - sigma))).astype(jnp.bfloat16)
    dup = (dact * gate * sigma).astype(jnp.bfloat16)
    full = gather_row(jnp.concatenate([act, dgate, dup], axis=1))
    act_full = full[:, :width]
    dgate_full = full[:, width : 2 * width]
    dup_full = full[:, 2 * width :]
    out_partials = jnp.concatenate(
        [
            product(act_full, masked_down).astype(jnp.bfloat16),
            product_t(full[:, width:], gate_up).astype(
                jnp.bfloat16
            ),
        ],
        axis=1,
    )
    outs = reduce_col(out_partials).astype(jnp.bfloat16)
    layer_out = outs[:, :feat]
    token_grad = outs[:, feat:]
    scale = total_rows ** (-0.5)
    gate_grad = masked(contract_rows(panel, dgate_full) * scale, block_mask[0]).astype(jnp.bfloat16)
    up_grad = masked(contract_rows(panel, dup_full) * scale, block_mask[1]).astype(jnp.bfloat16)
    down_grad = masked(contract_rows(act_full, grad_panel) * scale, block_mask[2].T).astype(
        jnp.bfloat16
    )
    return (layer_out, token_grad, gate_grad, up_grad, down_grad)


def solution(mesh):
    n_row, n_col = mesh.devices.shape
    fine = Mesh(mesh.devices.reshape(n_row // 2, 2, 4, n_col // 4), ("x", "core", "y", "z"))
    in_specs = (
        P(COL, ROW),
        P(COL, ROW),
        P(ROW, COL),
        P(ROW, COL),
        P(COL, ROW),
        P(None, ROW, COL),
    )
    out_specs = (
        P(COL, ROW),
        P(COL, ROW),
        P(ROW, COL),
        P(ROW, COL),
        P(COL, ROW),
    )
    return jax.shard_map(shards, mesh=fine, in_specs=in_specs, out_specs=out_specs, check_vma=False)
```

```python
import jax
import jax.numpy as jnp
from jax import lax
from jax.sharding import Mesh
from jax.sharding import PartitionSpec as P

COL = ("y", "z")
ROW = ("x", "core")


def masked(weight, mask):
    rows, cols = mask.shape
    shaped = weight.reshape(rows, weight.shape[0] // rows, cols, weight.shape[1] // cols)
    return (shaped * mask.astype(weight.dtype)[:, None, :, None]).reshape(weight.shape)


def product(left, weight):
    return jnp.dot(left, weight, preferred_element_type=jnp.float32)


def product_t(left, weight):
    return lax.dot_general(
        left, weight, (((1,), (1,)), ((), ())), preferred_element_type=jnp.float32
    )


def contract_rows(left, right):
    return lax.dot_general(
        left, right, (((0,), (0,)), ((), ())), preferred_element_type=jnp.float32
    )


def add_blocks(got):
    total = got[0].astype(jnp.float32)
    for i in range(1, got.shape[0]):
        total = total + got[i].astype(jnp.float32)
    return total


def gather_rows(local, axis):
    size = lax.axis_size(axis)
    sent = jnp.broadcast_to(local[None], (size,) + local.shape)
    got = lax.all_to_all(sent, axis, 0, 0, tiled=False)
    return got.reshape((size * local.shape[0],) + local.shape[1:])


def reduce_rows(partial, axis):
    size = lax.axis_size(axis)
    chunks = partial.astype(jnp.bfloat16).reshape((size, partial.shape[0] // size) + partial.shape[1:])
    got = lax.all_to_all(chunks, axis, 0, 0, tiled=False)
    return add_blocks(got)


def permute_gather(local, axis):
    size = lax.axis_size(axis)
    me = lax.axis_index(axis)
    got = [local] + [
        lax.ppermute(local, axis, [(i, (i + k) % size) for i in range(size)]) for k in range(1, size)
    ]
    order = (me - jnp.arange(size)) % size
    return jnp.take(jnp.stack(got), order, axis=0).reshape((size * local.shape[0],) + local.shape[1:])


def gather_col(local):
    return gather_rows(permute_gather(local, "z"), "y")


def reduce_col(partial):
    return reduce_rows(reduce_rows(partial, "y"), "z")


def reduce_row(partial):
    n_x = lax.axis_size("x")
    n_core = lax.axis_size("core")
    rows = partial.shape[0] // (n_x * n_core)
    split = partial.astype(jnp.bfloat16).reshape((n_core, n_x, rows) + partial.shape[1:])
    got = add_blocks(lax.all_to_all(split, "core", 0, 0, tiled=False))
    return add_blocks(lax.all_to_all(got.astype(jnp.bfloat16), "x", 0, 0, tiled=False))


def gather_row(local):
    n_x = lax.axis_size("x")
    n_core = lax.axis_size("core")
    over_x = gather_rows(local, "x").reshape((n_x,) + local.shape)
    sent = jnp.broadcast_to(over_x[None], (n_core,) + over_x.shape)
    both = lax.all_to_all(sent, "core", 0, 0, tiled=False)
    return both.reshape((n_core * n_x * local.shape[0],) + local.shape[1:])


def shards(tokens, cotangent, gate_weight, up_weight, down_weight, block_mask):
    masked_gate = masked(gate_weight, block_mask[0])
    masked_up = masked(up_weight, block_mask[1])
    masked_down = masked(down_weight, block_mask[2].T)
    feat = tokens.shape[1]
    both = gather_col(jnp.concatenate([tokens, cotangent], axis=1))
    panel = both[:, :feat]
    grad_panel = both[:, feat:]
    total_rows = panel.shape[0]
    width = masked_gate.shape[1]
    partials = jnp.concatenate(
        [
            product(panel, masked_gate).astype(jnp.bfloat16),
            product(panel, masked_up).astype(jnp.bfloat16),
            product_t(grad_panel, masked_down).astype(jnp.bfloat16),
        ],
        axis=1,
    )
    sums = reduce_row(partials)
    gate = sums[:, :width]
    up = sums[:, width : 2 * width]
    dact = sums[:, 2 * width :]
    sigma = jax.nn.sigmoid(gate)
    act = (gate * sigma * up).astype(jnp.bfloat16)
    dgate = (dact * up * sigma * (1.0 + gate * (1.0 - sigma))).astype(jnp.bfloat16)
    dup = (dact * gate * sigma).astype(jnp.bfloat16)
    full = gather_row(jnp.concatenate([act, dgate, dup], axis=1))
    act_full = full[:, :width]
    dgate_full = full[:, width : 2 * width]
    dup_full = full[:, 2 * width :]
    out_partials = jnp.concatenate(
        [
            product(act_full, masked_down).astype(jnp.bfloat16),
            product_t(full[:, width:], jnp.concatenate([masked_gate, masked_up], axis=1)).astype(
                jnp.bfloat16
            ),
        ],
        axis=1,
    )
    outs = reduce_col(out_partials).astype(jnp.bfloat16)
    layer_out = outs[:, :feat]
    token_grad = outs[:, feat:]
    scale = total_rows ** (-0.5)
    gate_grad = masked(contract_rows(panel, dgate_full) * scale, block_mask[0]).astype(jnp.bfloat16)
    up_grad = masked(contract_rows(panel, dup_full) * scale, block_mask[1]).astype(jnp.bfloat16)
    down_grad = masked(contract_rows(act_full, grad_panel) * scale, block_mask[2].T).astype(
        jnp.bfloat16
    )
    return (layer_out, token_grad, gate_grad, up_grad, down_grad)


def solution(mesh):
    n_row, n_col = mesh.devices.shape
    fine = Mesh(mesh.devices.reshape(n_row // 2, 2, 4, n_col // 4), ("x", "core", "y", "z"))
    in_specs = (
        P(COL, ROW),
        P(COL, ROW),
        P(ROW, COL),
        P(ROW, COL),
        P(COL, ROW),
        P(None, ROW, COL),
    )
    out_specs = (
        P(COL, ROW),
        P(COL, ROW),
        P(ROW, COL),
        P(ROW, COL),
        P(COL, ROW),
    )
    return jax.shard_map(shards, mesh=fine, in_specs=in_specs, out_specs=out_specs, check_vma=False)
```
